256 devices in a mesh: dp: 8 (over x, core), expert: 32 (over y, z).
Axes of the slice: x: 4, y: 4, z: 8, core: 2. Of those that a mesh axis runs over, the one named last changes fastest.
Arguments:
- tokens: bfloat16 [8192, 2048], P(('dp', 'expert')), may hold values from -6 to 6
- expert_ids: int32 [8192, 8], P(('dp', 'expert')), may hold values from 0 to 31, all different within a row; in each aligned block of 32 rows (0 to 31, 32 to 63, ...) at most 16 rows name the same one
- gate_weights: float32 [8192, 8], P(('dp', 'expert')), may hold values from 0.05 to 0.35
- grad_output: bfloat16 [8192, 2048], P(('dp', 'expert')), may hold values from -6 to 6
- w_gate_up: bfloat16 [32, 2048, 1536], P('expert'), may hold values from -0.125 to 0.125
- w_down: bfloat16 [32, 768, 2048], P('expert'), may hold values from -0.21875 to 0.21875
Outputs:
- mixed: bfloat16 [8192, 2048], P(('dp', 'expert'))
- grad_tokens: bfloat16 [8192, 2048], P(('dp', 'expert'))
- grad_gates: float32 [8192, 8], P(('dp', 'expert'))
- grad_gate_up: float32 [32, 2048, 1536], P('expert', 'dp')
- grad_down: float32 [32, 768, 2048], P('expert', None, 'dp')
The draws below stay inside these ranges and needn't reach their ends.
Inputs may be any that keep to these rules, and one draw needn't show every extreme that they name: `expert_ids`: in each block of 32 rows (the rows of one device) every expert is named at most 16 times, a bound that some block reaches; a row names 8 different experts, and every expert is named somewhere.
All inputs are finite; a program needn't handle non-finite values.
Results may differ from the reference program's by a relative error of at most 0.015.
Values may be sent and summed in bfloat16 or wider, within the bound.
No kernel may reach another device: no remote copies, remote signals or barrier semaphores. Data moves between devices by JAX's collectives and lax.ppermute only.
A program may use at most 128 MiB of HBM per device.

```python
import math
import jax
import jax.numpy as jnp
import numpy as np
from jax import lax

D = 2048
FF = 768
TOPK = 8
TOK_DEV = 32
EXPERTS = 32
CAP = 16
TOKENS = 8192
N_DP = 8
N_EXPERT = 32


def steps_of(stream_key, dims, shards, low, top_value):
    level = 1.0
    for dim, parts in shards:
        heights = jax.random.uniform(jax.random.fold_in(jax.random.fold_in(stream_key, 6), dim), (parts,), jnp.float32, low / len(shards), top_value / len(shards))
        level = level * jnp.repeat(jnp.exp(heights), dims[dim] // parts).reshape((-1,) + (1,) * (len(dims) - 1 - dim))
    return level


def deal_out(own_key, own, number, rows, number_of, top, most, lean):
    ranking = jax.random.permutation(own_key, number_of)
    heavy_load, usual = load_shares(number_of, rows * top, most, lean, True), load_shares(number_of, rows * top, most, lean, False)
    places = jnp.arange(number_of)

    def named(sizes, turn):
        used = int((sizes > 0).sum())
        fixed = max(1, used // 4)
        moved = fixed + (places - fixed + turn * (used - fixed)) % max(1, number_of - fixed)
        return jnp.zeros((number_of,), jnp.int32).at[ranking[jnp.where(places < fixed, places, moved)]].set(jnp.asarray(sizes, jnp.int32))

    sizes = jnp.where(number % 4 == 0, named(heavy_load, number // 4), named(usual, number - number // 4 - 1))
    mixed = jax.random.permutation(jax.random.fold_in(own, 3), number_of)
    giver, sink = mixed[0:number_of // 2 * 2:2], mixed[1:number_of // 2 * 2:2]
    margin = jnp.minimum(sizes[giver] - 1, most - sizes[sink]) // 2
    margin = jnp.where((giver == ranking[0]) | (sink == ranking[0]) | (sizes[sink] == 0), 0, jnp.maximum(margin, 0))
    moved = jax.random.randint(jax.random.fold_in(own, 4), (number_of // 2,), 0, 1 << 20) % (margin + 1)
    sizes = sizes.at[giver].add(-moved).at[sink].add(moved)
    members = jnp.searchsorted(jnp.cumsum(sizes), jnp.arange(rows * top), side="right").astype(jnp.int32)
    grid = members.reshape(top, rows).T
    grid = grid[jax.random.permutation(jax.random.fold_in(own, 1), rows)]
    turn = jax.random.randint(jax.random.fold_in(own, 2), (rows, 1), 0, top)
    return jnp.take_along_axis(grid, (jnp.arange(top)[None, :] + turn) % top, axis=1)


def load_shares(amount, total, most, skew, full):
    portions = [(1 << 20) // math.isqrt(rank ** skew) + 1 for rank in range(1, amount + 1)]
    largest = most if full else min(most, max(-(-total // amount), total * portions[0] // sum(portions)))
    least = 1 if total - largest >= amount - 1 else 0
    given, rest = [largest] + [least] * (amount - 1), total - largest - least * (amount - 1)
    while rest > 0:
        free = [i for i in range(1, amount) if given[i] < largest] or [i for i in range(1, amount) if given[i] < most]
        whole, budget = sum([portions[i] for i in free]), rest
        for i in free:
            addition = min(most - given[i], max(1, budget * portions[i] // whole), rest)
            given[i] = given[i] + addition
            rest = rest - addition
    return np.array(given)


def noise(own_key, dims, width, reach, shards=(), kind=jnp.bfloat16):
    gain = steps_of(own_key, dims, shards, -0.22, 0.18) if shards else 1.0
    result = jax.random.normal(own_key, dims, jnp.float32) * width * gain
    return jnp.minimum(jnp.maximum(result, -reach), reach).astype(kind)


def setup_inputs(seed: int = 0) -> dict:
    key_of = jax.random.split(jax.random.key(seed), 7)
    tokens = noise(key_of[0], (TOKENS, D), 1.0, 6.0, ((0, 256),))
    expert_ids_keys = jax.random.split(jax.random.fold_in(key_of[1], 1), TOKENS // TOK_DEV)
    expert_ids_turns = jax.random.permutation(jax.random.fold_in(key_of[1], 3), TOKENS // TOK_DEV)
    expert_ids = jax.vmap(lambda own, number: deal_out(jax.random.fold_in(key_of[1], 2), own, number, TOK_DEV, EXPERTS, TOPK, CAP, 2))(expert_ids_keys, expert_ids_turns).reshape((TOKENS, TOPK))
    gate_weights = jnp.clip(0.05 + 0.29999999 * jax.random.uniform(key_of[2], (TOKENS, TOPK), jnp.float32) ** steps_of(key_of[2], (TOKENS, TOPK), ((0, 256),), -0.2, 0.2), 0.05, 0.35)
    grad_output = noise(key_of[3], (TOKENS, D), 1.0, 6.0, ((0, 256),))
    w_gate_up = noise(key_of[4], (EXPERTS, D, 2 * FF), D ** -0.5, 0.125, ((0, 32),))
    w_down = noise(key_of[5], (EXPERTS, FF, D), FF ** -0.5, 0.21875, ((0, 32),))
    return dict(tokens=tokens, expert_ids=expert_ids, gate_weights=gate_weights, grad_output=grad_output, w_gate_up=w_gate_up, w_down=w_down)


def swish_parts(gate_up):
    gate_half = gate_up[..., :FF]
    up_half = gate_up[..., FF:]
    sigmoid_part = jax.nn.sigmoid(gate_half)
    return gate_half, up_half, sigmoid_part


def reference(tokens, expert_ids, gate_weights, grad_output, w_gate_up, w_down):
    device_count = N_DP * N_EXPERT
    pair_count = TOK_DEV * TOPK
    pair_total = TOKENS * TOPK
    ids_blocks = expert_ids.reshape(device_count, pair_count)
    onehot = (ids_blocks[:, :, None] == jnp.arange(EXPERTS, dtype=jnp.int32)[None, None, :]).astype(jnp.int32)
    before = jnp.cumsum(onehot, axis=1) - onehot
    slots = jnp.sum(before * onehot, axis=2).reshape(-1).astype(jnp.int32)
    flat_ids = expert_ids.reshape(-1)
    flat_gates = gate_weights.reshape(-1)
    pair_index = jnp.arange(pair_total, dtype=jnp.int32)
    pair_device = pair_index // pair_count
    buffer_rows = device_count * CAP
    row_index = pair_device * CAP + slots

    def per_expert(carry, inputs):
        mixed_sum, token_grad, gate_grad = carry
        expert, weight_gu, weight_down = inputs
        target = jnp.where(flat_ids == expert, row_index, buffer_rows)
        source_pair = jnp.full((buffer_rows,), pair_total, jnp.int32).at[target].set(pair_index, mode="drop")
        filled = source_pair < pair_total
        safe_pair = jnp.where(filled, source_pair, 0)
        source_token = safe_pair // TOPK
        xrows = jnp.where(filled[:, None], tokens[source_token], jnp.zeros((), jnp.bfloat16))
        row_gate = jnp.where(filled, flat_gates[safe_pair], jnp.zeros((), jnp.float32))
        gate_up = jnp.dot(xrows, weight_gu, preferred_element_type=jnp.float32)
        gate_half, up_half, sigmoid_part = swish_parts(gate_up)
        swish = gate_half * sigmoid_part
        hidden = (swish * up_half).astype(jnp.bfloat16)
        out_rows = jnp.dot(hidden, weight_down, preferred_element_type=jnp.float32).astype(jnp.bfloat16)
        dy_rows = grad_output[source_token]
        pair_grad = jnp.sum(out_rows.astype(jnp.float32) * dy_rows.astype(jnp.float32), axis=1)
        grad_rows = (row_gate[:, None] * dy_rows.astype(jnp.float32)).astype(jnp.bfloat16)
        grad_hidden = jnp.dot(grad_rows, weight_down.T, preferred_element_type=jnp.float32)
        grad_gate = grad_hidden * up_half * sigmoid_part * (1.0 + gate_half * (1.0 - sigmoid_part))
        grad_up = grad_hidden * swish
        grad_act = jnp.concatenate([grad_gate, grad_up], axis=1).astype(jnp.bfloat16)
        grad_in = jnp.dot(grad_act, weight_gu.T, preferred_element_type=jnp.float32).astype(jnp.bfloat16)
        token_target = jnp.where(filled, source_token, TOKENS)
        mixed_sum = mixed_sum.at[token_target].add(row_gate[:, None] * out_rows.astype(jnp.float32), mode="drop")
        token_grad = token_grad.at[token_target].add(grad_in.astype(jnp.float32), mode="drop")
        gate_grad = gate_grad.at[jnp.where(filled, source_pair, pair_total)].set(pair_grad, mode="drop")
        group_x = xrows.reshape(N_DP, -1, D).astype(jnp.float32)
        group_act = grad_act.reshape(N_DP, -1, 2 * FF).astype(jnp.float32)
        group_hidden = hidden.reshape(N_DP, -1, FF).astype(jnp.float32)
        group_grad = grad_rows.reshape(N_DP, -1, D).astype(jnp.float32)
        part_gu = jnp.einsum("grd,grf->gdf", group_x, group_act).astype(jnp.bfloat16)
        part_gu = lax.optimization_barrier(part_gu)
        part_down = jnp.einsum("grf,grd->gfd", group_hidden, group_grad).astype(jnp.bfloat16)
        part_down = lax.optimization_barrier(part_down)
        total_gu = jnp.sum(part_gu.astype(jnp.float32), axis=0)
        total_down = jnp.sum(part_down.astype(jnp.float32), axis=0)
        return (mixed_sum, token_grad, gate_grad), (total_gu, total_down)

    start = (jnp.zeros((TOKENS, D), jnp.float32), jnp.zeros((TOKENS, D), jnp.float32), jnp.zeros((pair_total,), jnp.float32))
    experts_list = jnp.arange(EXPERTS, dtype=jnp.int32)
    (mixed_sum, token_grad, gate_grad), (grad_gate_up, grad_down) = lax.scan(per_expert, start, (experts_list, w_gate_up, w_down))
    return (mixed_sum.astype(jnp.bfloat16), token_grad.astype(jnp.bfloat16), gate_grad.reshape(TOKENS, TOPK), grad_gate_up, grad_down)
```

```python
import jax
import jax.numpy as jnp
from jax import lax
from jax.sharding import PartitionSpec as P


def swish_parts(gate_up, hidden_units):
    gate_half = gate_up[..., :hidden_units]
    up_half = gate_up[..., hidden_units:]
    sigmoid_part = jax.nn.sigmoid(gate_half)
    return (gate_half, up_half, sigmoid_part)


def body(tokens, expert_ids, gate_weights, grad_output, w_gate_up, w_down):
    token_count, top_count = expert_ids.shape
    width = tokens.shape[1]
    per_device = w_gate_up.shape[0]
    hidden_units = w_down.shape[1]
    owners = lax.axis_size("expert")
    expert_total = owners * per_device
    capacity = min(token_count, 2 * token_count * top_count // expert_total)
    pair_count = token_count * top_count
    me = lax.axis_index("expert")

    all_tokens = lax.all_gather(tokens, "expert", tiled=True).reshape(owners, token_count, width)
    all_ids = lax.all_gather(expert_ids, "expert", tiled=True).reshape(owners, pair_count)
    all_gates = lax.all_gather(gate_weights, "expert", tiled=True).reshape(owners, pair_count)
    all_grad = lax.all_gather(grad_output, "expert", tiled=True).reshape(owners, token_count, width)

    local_experts = me * per_device + jnp.arange(per_device, dtype=jnp.int32)
    onehot = all_ids[:, :, None] == local_experts[None, None, :]
    onehot_i = onehot.astype(jnp.int32)
    slots = jnp.cumsum(onehot_i, axis=1) - onehot_i
    slot_axis = jnp.arange(capacity, dtype=jnp.int32)
    sel = jnp.logical_and(onehot[..., None], slots[..., None] == slot_axis).transpose(2, 0, 3, 1)
    sel_f = sel.astype(jnp.float32)
    row_gate = jnp.sum(sel_f * all_gates[None, :, None, :], axis=3)
    sel_tok = jnp.sum(
        sel.reshape(per_device, owners, capacity, token_count, top_count).astype(jnp.bfloat16),
        axis=4,
    )

    x_rows = jnp.einsum(
        "jsct,std->jscd", sel_tok, all_tokens, preferred_element_type=jnp.float32
    ).astype(jnp.bfloat16)
    dy_rows = jnp.einsum(
        "jsct,std->jscd", sel_tok, all_grad, preferred_element_type=jnp.float32
    )
    x_rows = x_rows.reshape(per_device, owners * capacity, width)
    dy_rows = dy_rows.reshape(per_device, owners * capacity, width)
    row_gate = row_gate.reshape(per_device, owners * capacity)

    gate_up = jnp.einsum("jrd,jdf->jrf", x_rows, w_gate_up, preferred_element_type=jnp.float32)
    gate_half, up_half, sigmoid_part = swish_parts(gate_up, hidden_units)
    swish = gate_half * sigmoid_part
    hidden = (swish * up_half).astype(jnp.bfloat16)
    out_rows = jnp.einsum(
        "jrf,jfd->jrd", hidden, w_down, preferred_element_type=jnp.float32
    ).astype(jnp.bfloat16)

    grad_rows = (row_gate[..., None] * dy_rows).astype(jnp.bfloat16)
    grad_hidden = jnp.einsum("jrd,jfd->jrf", grad_rows, w_down, preferred_element_type=jnp.float32)
    grad_gate = grad_hidden * up_half * sigmoid_part * (1.0 + gate_half * (1.0 - sigmoid_part))
    grad_up = grad_hidden * swish
    grad_act = jnp.concatenate([grad_gate, grad_up], axis=2).astype(jnp.bfloat16)
    grad_in = jnp.einsum(
        "jrf,jdf->jrd", grad_act, w_gate_up, preferred_element_type=jnp.float32
    ).astype(jnp.bfloat16)

    out_f = out_rows.astype(jnp.float32)
    row_inner = jnp.sum(out_f * dy_rows, axis=2).reshape(per_device, owners, capacity)
    gate_part = jnp.sum(sel_f * row_inner[..., None], axis=(0, 2)).reshape(owners * token_count, top_count)
    weighted = (row_gate[..., None] * out_f).astype(jnp.bfloat16)
    mixed_part = jnp.einsum(
        "jsct,jscd->std",
        sel_tok,
        weighted.reshape(per_device, owners, capacity, width),
        preferred_element_type=jnp.float32,
    ).astype(jnp.bfloat16)
    mixed = lax.psum_scatter(
        mixed_part.reshape(owners * token_count, width), "expert", scatter_dimension=0, tiled=True
    )
    grad_gates = lax.psum_scatter(gate_part, "expert", scatter_dimension=0, tiled=True)
    tokens_part = jnp.einsum(
        "jsct,jscd->std",
        sel_tok,
        grad_in.reshape(per_device, owners, capacity, width),
        preferred_element_type=jnp.float32,
    ).astype(jnp.bfloat16)
    grad_tokens = lax.psum_scatter(
        tokens_part.reshape(owners * token_count, width), "expert", scatter_dimension=0, tiled=True
    )

    down_local = jnp.einsum("jrf,jrd->jfd", hidden, grad_rows, preferred_element_type=jnp.float32)
    gate_up_local = jnp.einsum("jrd,jrf->jdf", x_rows, grad_act, preferred_element_type=jnp.float32)
    grad_gate_up = lax.psum_scatter(
        gate_up_local.astype(jnp.bfloat16), "dp", scatter_dimension=1, tiled=True
    ).astype(jnp.float32)
    grad_down = lax.psum_scatter(
        down_local.astype(jnp.bfloat16), "dp", scatter_dimension=2, tiled=True
    ).astype(jnp.float32)
    return (mixed, grad_tokens, grad_gates, grad_gate_up, grad_down)


def solution(mesh):
    in_specs = (
        P(("dp", "expert"), None),
        P(("dp", "expert"), None),
        P(("dp", "expert"), None),
        P(("dp", "expert"), None),
        P("expert", None, None),
        P("expert", None, None),
    )
    out_specs = (
        P(("dp", "expert"), None),
        P(("dp", "expert"), None),
        P(("dp", "expert"), None),
        P("expert", "dp", None),
        P("expert", None, "dp"),
    )
    return jax.shard_map(body, mesh=mesh, in_specs=in_specs, out_specs=out_specs, check_vma=False)
```

```python
import jax
import jax.numpy as jnp
from jax import lax
from jax.sharding import Mesh
from jax.sharding import PartitionSpec as P


def swish_parts(gate_up, hidden_units):
    gate_half = gate_up[..., :hidden_units]
    up_half = gate_up[..., hidden_units:]
    sigmoid_part = jax.nn.sigmoid(gate_half)
    return (gate_half, up_half, sigmoid_part)


def ring_offsets(n):
    half = n // 2
    return list(range(-half, n - half))


def ring_gather(x, axis, n):
    right = [(i, (i + 1) % n) for i in range(n)]
    left = [(i, (i - 1) % n) for i in range(n)]
    half = n // 2
    got = {0: x}
    fwd, bwd = x, x
    for k in range(1, half + 1):
        fwd = lax.ppermute(fwd, axis, right)
        got[-k] = fwd
        if k <= n - half - 1:
            bwd = lax.ppermute(bwd, axis, left)
            got[k] = bwd
    return jax.tree.map(lambda *xs: jnp.stack(xs), *[got[o] for o in ring_offsets(n)])


def ring_reduce(parts, axis, n, send_dtypes):
    right = [(i, (i + 1) % n) for i in range(n)]
    left = [(i, (i - 1) % n) for i in range(n)]
    half = n // 2
    index = {o: i for i, o in enumerate(ring_offsets(n))}

    def pick(o):
        return tuple(p[index[o]] for p in parts)

    def send(acc, perm):
        sent = lax.ppermute(tuple(a.astype(t) for a, t in zip(acc, send_dtypes)), axis, perm)
        return tuple(s.astype(jnp.float32) for s in sent)

    def add(a, b):
        return tuple(x + y for x, y in zip(a, b))

    total = pick(0)
    acc = pick(-half)
    for t in range(1, half):
        acc = add(send(acc, left), pick(-half + t))
    total = add(total, send(acc, left))
    m = n - half - 1
    if m > 0:
        acc = pick(m)
        for t in range(1, m):
            acc = add(send(acc, right), pick(m - t))
        total = add(total, send(acc, right))
    return total


def body(tokens, expert_ids, gate_weights, grad_output, w_gate_up, w_down):
    token_count, top_count = expert_ids.shape
    width = tokens.shape[1]
    per_device = w_gate_up.shape[0]
    hidden_units = w_down.shape[1]
    ny = lax.axis_size("ey")
    nz = lax.axis_size("ez")
    expert_total = ny * nz * per_device
    capacity = min(token_count, 2 * token_count * top_count // expert_total)
    pair_count = token_count * top_count
    my_z = lax.axis_index("ez")

    tok_g, dy_g, ids_g, gates_g = ring_gather(
        (tokens, grad_output, expert_ids, gate_weights), "ez", nz
    )
    nb = tok_g.shape[0]
    ids_g = ids_g.reshape(nb, pair_count)
    gates_g = gates_g.reshape(nb, pair_count)

    dest = (
        (jnp.arange(ny, dtype=jnp.int32)[:, None] * nz + my_z) * per_device
        + jnp.arange(per_device, dtype=jnp.int32)[None, :]
    )
    onehot = ids_g[None, None, :, :] == dest[:, :, None, None]
    onehot_i = onehot.astype(jnp.int32)
    slots = jnp.cumsum(onehot_i, axis=3) - onehot_i
    slot_axis = jnp.arange(capacity, dtype=jnp.int32)
    sel = jnp.logical_and(onehot[:, :, :, None, :], slots[:, :, :, None, :] == slot_axis[:, None])
    sel_f = sel.astype(jnp.float32)
    row_gate = jnp.sum(sel_f * gates_g[None, None, :, None, :], axis=4)
    sel_tok = jnp.sum(
        sel.reshape(ny, per_device, nb, capacity, token_count, top_count).astype(jnp.bfloat16),
        axis=5,
    )
    send_x = jnp.einsum(
        "yjoct,otd->yjocd", sel_tok, tok_g, preferred_element_type=jnp.float32
    ).astype(jnp.bfloat16)
    routed_dy = jnp.einsum("yjoct,otd->yjocd", sel_tok, dy_g, preferred_element_type=jnp.float32)
    send_g = (row_gate[..., None] * routed_dy).astype(jnp.bfloat16)

    def to_rows(a):
        return a.transpose(1, 0, 2, 3, 4).reshape(per_device, ny * nb * capacity, width)

    def from_rows(a):
        return a.reshape(per_device, ny, nb, capacity, width).transpose(1, 0, 2, 3, 4)

    x_rows = to_rows(lax.all_to_all(send_x, "ey", 0, 0, tiled=True))
    gate_up = jnp.einsum("jrd,jdf->jrf", x_rows, w_gate_up, preferred_element_type=jnp.float32)
    gate_half, up_half, sigmoid_part = swish_parts(gate_up, hidden_units)
    swish = gate_half * sigmoid_part
    hidden = (swish * up_half).astype(jnp.bfloat16)
    out_rows = jnp.einsum(
        "jrf,jfd->jrd", hidden, w_down, preferred_element_type=jnp.float32
    ).astype(jnp.bfloat16)
    back_out = lax.all_to_all(from_rows(out_rows), "ey", 0, 0, tiled=True)

    grad_rows = to_rows(lax.all_to_all(send_g, "ey", 0, 0, tiled=True))
    grad_hidden = jnp.einsum("jrd,jfd->jrf", grad_rows, w_down, preferred_element_type=jnp.float32)
    grad_gate = grad_hidden * up_half * sigmoid_part * (1.0 + gate_half * (1.0 - sigmoid_part))
    grad_up = grad_hidden * swish
    grad_act = jnp.concatenate([grad_gate, grad_up], axis=2).astype(jnp.bfloat16)
    grad_in = jnp.einsum(
        "jrf,jdf->jrd", grad_act, w_gate_up, preferred_element_type=jnp.float32
    ).astype(jnp.bfloat16)
    back_in = lax.all_to_all(from_rows(grad_in), "ey", 0, 0, tiled=True)

    back_f = back_out.astype(jnp.float32)
    row_inner = jnp.sum(back_f * routed_dy, axis=4)
    gate_part = jnp.sum(sel_f * row_inner[..., None], axis=(0, 1, 3)).reshape(nb, token_count, top_count)
    mixed_part = jnp.einsum(
        "yjoct,yjocd->otd",
        sel_tok.astype(jnp.float32),
        row_gate[..., None] * back_f,
        precision=lax.Precision.HIGHEST,
        preferred_element_type=jnp.float32,
    )
    mixed, grad_gates = ring_reduce((mixed_part, gate_part), "ez", nz, (jnp.bfloat16, jnp.float32))
    tokens_part = jnp.einsum("yjoct,yjocd->otd", sel_tok, back_in, preferred_element_type=jnp.float32)
    (grad_tokens,) = ring_reduce((tokens_part,), "ez", nz, (jnp.bfloat16,))

    down_local = jnp.einsum("jrf,jrd->jfd", hidden, grad_rows, preferred_element_type=jnp.float32)
    gate_up_local = jnp.einsum("jrd,jrf->jdf", x_rows, grad_act, preferred_element_type=jnp.float32)
    grad_gate_up = lax.psum_scatter(
        gate_up_local.astype(jnp.bfloat16), "dp", scatter_dimension=1, tiled=True
    ).astype(jnp.float32)
    grad_down = lax.psum_scatter(
        down_local.astype(jnp.bfloat16), "dp", scatter_dimension=2, tiled=True
    ).astype(jnp.float32)
    return (
        mixed.astype(jnp.bfloat16),
        grad_tokens.astype(jnp.bfloat16),
        grad_gates,
        grad_gate_up,
        grad_down,
    )


def solution(mesh):
    ny = mesh.devices.shape[1] // 8 if mesh.devices.shape[1] % 8 == 0 else 1
    nz = mesh.devices.shape[1] // ny
    split = Mesh(mesh.devices.reshape(mesh.devices.shape[0], ny, nz), ("dp", "ey", "ez"))
    rows = ("dp", "ey", "ez")
    experts = ("ey", "ez")
    in_specs = (
        P(rows, None),
        P(rows, None),
        P(rows, None),
        P(rows, None),
        P(experts, None, None),
        P(experts, None, None),
    )
    out_specs = (
        P(rows, None),
        P(rows, None),
        P(rows, None),
        P(experts, "dp", None),
        P(experts, None, "dp"),
    )
    return jax.shard_map(body, mesh=split, in_specs=in_specs, out_specs=out_specs, check_vma=False)
```

```python
import jax
import jax.numpy as jnp
from jax import lax
from jax.sharding import Mesh
from jax.sharding import PartitionSpec as P


def swish_parts(gate_up, hidden_units):
    gate_half = gate_up[..., :hidden_units]
    up_half = gate_up[..., hidden_units:]
    sigmoid_part = jax.nn.sigmoid(gate_half)
    return (gate_half, up_half, sigmoid_part)


def ring_offsets(n):
    half = n // 2
    return list(range(-half, n - half))


def ring_gather(x, axis, n):
    right = [(i, (i + 1) % n) for i in range(n)]
    left = [(i, (i - 1) % n) for i in range(n)]
    half = n // 2
    got = {0: x}
    fwd, bwd = x, x
    for k in range(1, half + 1):
        fwd = lax.ppermute(fwd, axis, right)
        got[-k] = fwd
        if k <= n - half - 1:
            bwd = lax.ppermute(bwd, axis, left)
            got[k] = bwd
    return jax.tree.map(lambda *xs: jnp.stack(xs), *[got[o] for o in ring_offsets(n)])


def ring_reduce(parts, axis, n, send_dtypes):
    right = [(i, (i + 1) % n) for i in range(n)]
    left = [(i, (i - 1) % n) for i in range(n)]
    half = n // 2
    index = {o: i for i, o in enumerate(ring_offsets(n))}

    def pick(o):
        return tuple(p[index[o]] for p in parts)

    def send(acc, perm):
        sent = lax.ppermute(tuple(a.astype(t) for a, t in zip(acc, send_dtypes)), axis, perm)
        return tuple(s.astype(jnp.float32) for s in sent)

    def add(a, b):
        return tuple(x + y for x, y in zip(a, b))

    total = pick(0)
    acc = pick(-half)
    for t in range(1, half):
        acc = add(send(acc, left), pick(-half + t))
    total = add(total, send(acc, left))
    m = n - half - 1
    if m > 0:
        acc = pick(m)
        for t in range(1, m):
            acc = add(send(acc, right), pick(m - t))
        total = add(total, send(acc, right))
    return total


def body(tokens, expert_ids, gate_weights, grad_output, w_gate_up, w_down):
    token_count, top_count = expert_ids.shape
    width = tokens.shape[1]
    per_device = w_gate_up.shape[0]
    hidden_units = w_down.shape[1]
    ny = lax.axis_size("ey")
    nz = lax.axis_size("ez")
    expert_total = ny * nz * per_device
    capacity = min(token_count, 2 * token_count * top_count // expert_total)
    pair_count = token_count * top_count
    my_z = lax.axis_index("ez")

    both_g = ring_gather(jnp.concatenate([tokens, grad_output], axis=1), "ez", nz)
    tok_g = both_g[..., :width]
    dy_g = both_g[..., width:]
    nb = both_g.shape[0]
    half = nz // 2
    meta = jnp.concatenate([expert_ids.astype(jnp.float32), gate_weights], axis=1)
    meta_abs = lax.all_to_all(jnp.broadcast_to(meta[None], (nz,) + meta.shape), "ez", 0, 0, tiled=True)
    meta_g = jnp.take(meta_abs, (my_z + jnp.arange(nz, dtype=jnp.int32) - half) % nz, axis=0)
    ids_g = meta_g[..., :top_count].astype(jnp.int32).reshape(nb, pair_count)
    gates_g = meta_g[..., top_count:].reshape(nb, pair_count)

    dest = (
        (jnp.arange(ny, dtype=jnp.int32)[:, None] * nz + my_z) * per_device
        + jnp.arange(per_device, dtype=jnp.int32)[None, :]
    )
    onehot = ids_g[None, None, :, :] == dest[:, :, None, None]
    onehot_i = onehot.astype(jnp.int32)
    slots = jnp.cumsum(onehot_i, axis=3) - onehot_i
    slot_axis = jnp.arange(capacity, dtype=jnp.int32)
    sel = jnp.logical_and(onehot[:, :, :, None, :], slots[:, :, :, None, :] == slot_axis[:, None])
    sel_f = sel.astype(jnp.float32)
    row_gate = jnp.sum(sel_f * gates_g[None, None, :, None, :], axis=4)
    sel_tok = jnp.sum(
        sel.reshape(ny, per_device, nb, capacity, token_count, top_count).astype(jnp.bfloat16),
        axis=5,
    )
    send_x = jnp.einsum(
        "yjoct,otd->yjocd", sel_tok, tok_g, preferred_element_type=jnp.float32
    ).astype(jnp.bfloat16)
    routed_dy = jnp.einsum("yjoct,otd->yjocd", sel_tok, dy_g, preferred_element_type=jnp.float32)
    send_g = (row_gate[..., None] * routed_dy).astype(jnp.bfloat16)

    def to_rows(a):
        return a.transpose(1, 0, 2, 3, 4).reshape(per_device, ny * nb * capacity, width)

    def from_rows(a):
        return a.reshape(per_device, ny, nb, capacity, width).transpose(1, 0, 2, 3, 4)

    x_rows = to_rows(lax.all_to_all(send_x, "ey", 0, 0, tiled=True))
    gate_up = jnp.einsum("jrd,jdf->jrf", x_rows, w_gate_up, preferred_element_type=jnp.float32)
    gate_half, up_half, sigmoid_part = swish_parts(gate_up, hidden_units)
    swish = gate_half * sigmoid_part
    hidden = (swish * up_half).astype(jnp.bfloat16)
    out_rows = jnp.einsum(
        "jrf,jfd->jrd", hidden, w_down, preferred_element_type=jnp.float32
    ).astype(jnp.bfloat16)
    back_out = lax.all_to_all(from_rows(out_rows), "ey", 0, 0, tiled=True)

    grad_rows = to_rows(lax.all_to_all(send_g, "ey", 0, 0, tiled=True))
    grad_hidden = jnp.einsum("jrd,jfd->jrf", grad_rows, w_down, preferred_element_type=jnp.float32)
    grad_gate = grad_hidden * up_half * sigmoid_part * (1.0 + gate_half * (1.0 - sigmoid_part))
    grad_up = grad_hidden * swish
    grad_act = jnp.concatenate([grad_gate, grad_up], axis=2).astype(jnp.bfloat16)
    grad_in = jnp.einsum(
        "jrf,jdf->jrd", grad_act, w_gate_up, preferred_element_type=jnp.float32
    ).astype(jnp.bfloat16)
    back_in = lax.all_to_all(from_rows(grad_in), "ey", 0, 0, tiled=True)

    back_f = back_out.astype(jnp.float32)
    row_inner = jnp.sum(back_f * routed_dy, axis=4)
    gate_part = jnp.sum(sel_f * row_inner[..., None], axis=(0, 1, 3)).reshape(nb, token_count, top_count)
    mixed_part = jnp.einsum(
        "yjoct,yjocd->otd",
        sel_tok.astype(jnp.float32),
        row_gate[..., None] * back_f,
        precision=lax.Precision.HIGHEST,
        preferred_element_type=jnp.float32,
    )
    gate_abs = jnp.take(gate_part, (jnp.arange(nz, dtype=jnp.int32) - my_z + half) % nz, axis=0)
    grad_gates = jnp.sum(lax.all_to_all(gate_abs, "ez", 0, 0, tiled=True), axis=0)
    tokens_part = jnp.einsum("yjoct,yjocd->otd", sel_tok, back_in, preferred_element_type=jnp.float32)
    (both,) = ring_reduce(
        (jnp.concatenate([mixed_part, tokens_part], axis=2),), "ez", nz, (jnp.bfloat16,)
    )
    mixed = both[:, :width]
    grad_tokens = both[:, width:]

    down_local = jnp.einsum("jrf,jrd->jfd", hidden, grad_rows, preferred_element_type=jnp.float32)
    gate_up_local = jnp.einsum("jrd,jrf->jdf", x_rows, grad_act, preferred_element_type=jnp.float32)
    grad_gate_up = lax.psum_scatter(
        gate_up_local.astype(jnp.bfloat16), "dp", scatter_dimension=1, tiled=True
    ).astype(jnp.float32)
    grad_down = lax.psum_scatter(
        down_local.astype(jnp.bfloat16), "dp", scatter_dimension=2, tiled=True
    ).astype(jnp.float32)
    return (
        mixed.astype(jnp.bfloat16),
        grad_tokens.astype(jnp.bfloat16),
        grad_gates,
        grad_gate_up,
        grad_down,
    )


def solution(mesh):
    ny = mesh.devices.shape[1] // 8 if mesh.devices.shape[1] % 8 == 0 else 1
    nz = mesh.devices.shape[1] // ny
    split = Mesh(mesh.devices.reshape(mesh.devices.shape[0], ny, nz), ("dp", "ey", "ez"))
    rows = ("dp", "ey", "ez")
    experts = ("ey", "ez")
    in_specs = (
        P(rows, None),
        P(rows, None),
        P(rows, None),
        P(rows, None),
        P(experts, None, None),
        P(experts, None, None),
    )
    out_specs = (
        P(rows, None),
        P(rows, None),
        P(rows, None),
        P(experts, "dp", None),
        P(experts, None, "dp"),
    )
    return jax.shard_map(body, mesh=split, in_specs=in_specs, out_specs=out_specs, check_vma=False)
```

```python
import jax
import jax.numpy as jnp
from jax import lax
from jax.sharding import Mesh
from jax.sharding import PartitionSpec as P


def swish_parts(gate_up, hidden_units):
    gate_half = gate_up[..., :hidden_units]
    up_half = gate_up[..., hidden_units:]
    sigmoid_part = jax.nn.sigmoid(gate_half)
    return (gate_half, up_half, sigmoid_part)


def split3(x):
    hi = x.astype(jnp.bfloat16)
    rest = x - hi.astype(jnp.float32)
    mid = rest.astype(jnp.bfloat16)
    lo = (rest - mid.astype(jnp.float32)).astype(jnp.bfloat16)
    return [hi, mid, lo]


def join3(parts, width):
    parts = parts.astype(jnp.float32)
    return (parts[..., :width] + parts[..., width : 2 * width]) + parts[..., 2 * width : 3 * width]


def ring_offsets(n):
    half = n // 2
    return list(range(-half, n - half))


def ring_gather(x, axis, n):
    right = [(i, (i + 1) % n) for i in range(n)]
    left = [(i, (i - 1) % n) for i in range(n)]
    half = n // 2
    got = {0: x}
    fwd, bwd = x, x
    for k in range(1, half + 1):
        fwd = lax.ppermute(fwd, axis, right)
        got[-k] = fwd
        if k <= n - half - 1:
            bwd = lax.ppermute(bwd, axis, left)
            got[k] = bwd
    return jax.tree.map(lambda *xs: jnp.stack(xs), *[got[o] for o in ring_offsets(n)])


def ring_reduce(parts, axis, n, send_dtypes):
    right = [(i, (i + 1) % n) for i in range(n)]
    left = [(i, (i - 1) % n) for i in range(n)]
    half = n // 2
    index = {o: i for i, o in enumerate(ring_offsets(n))}

    def pick(o):
        return tuple(p[index[o]] for p in parts)

    def send(acc, perm):
        sent = lax.ppermute(tuple(a.astype(t) for a, t in zip(acc, send_dtypes)), axis, perm)
        return tuple(s.astype(jnp.float32) for s in sent)

    def add(a, b):
        return tuple(x + y for x, y in zip(a, b))

    total = pick(0)
    acc = pick(-half)
    for t in range(1, half):
        acc = add(send(acc, left), pick(-half + t))
    total = add(total, send(acc, left))
    m = n - half - 1
    if m > 0:
        acc = pick(m)
        for t in range(1, m):
            acc = add(send(acc, right), pick(m - t))
        total = add(total, send(acc, right))
    return total


def body(tokens, expert_ids, gate_weights, grad_output, w_gate_up, w_down):
    token_count, top_count = expert_ids.shape
    width = tokens.shape[1]
    per_device = w_gate_up.shape[0]
    hidden_units = w_down.shape[1]
    ny = lax.axis_size("ey")
    nz = lax.axis_size("ez")
    expert_total = ny * nz * per_device
    capacity = min(token_count, 2 * token_count * top_count // expert_total)
    pair_count = token_count * top_count
    my_z = lax.axis_index("ez")

    packed = jnp.concatenate(
        [tokens, grad_output, expert_ids.astype(jnp.bfloat16)] + split3(gate_weights), axis=1
    )
    both_g = ring_gather(packed, "ez", nz)
    tok_g = both_g[..., :width]
    dy_g = both_g[..., width : 2 * width]
    nb = both_g.shape[0]
    meta_g = both_g[..., 2 * width :].astype(jnp.float32)
    ids_g = meta_g[..., :top_count].astype(jnp.int32).reshape(nb, pair_count)
    gates_g = join3(meta_g[..., top_count:], top_count).reshape(nb, pair_count)

    dest = (
        (jnp.arange(ny, dtype=jnp.int32)[:, None] * nz + my_z) * per_device
        + jnp.arange(per_device, dtype=jnp.int32)[None, :]
    )
    onehot = ids_g[None, None, :, :] == dest[:, :, None, None]
    onehot_i = onehot.astype(jnp.int32)
    slots = jnp.cumsum(onehot_i, axis=3) - onehot_i
    slot_axis = jnp.arange(capacity, dtype=jnp.int32)
    sel = jnp.logical_and(onehot[:, :, :, None, :], slots[:, :, :, None, :] == slot_axis[:, None])
    sel_f = sel.astype(jnp.float32)
    row_gate = jnp.sum(sel_f * gates_g[None, None, :, None, :], axis=4)
    sel_tok = jnp.sum(
        sel.reshape(ny, per_device, nb, capacity, token_count, top_count).astype(jnp.bfloat16),
        axis=5,
    )
    send_x = jnp.einsum(
        "yjoct,otd->yjocd", sel_tok, tok_g, preferred_element_type=jnp.float32
    ).astype(jnp.bfloat16)
    routed_dy = jnp.einsum("yjoct,otd->yjocd", sel_tok, dy_g, preferred_element_type=jnp.float32)
    send_g = (row_gate[..., None] * routed_dy).astype(jnp.bfloat16)

    def to_rows(a):
        return a.transpose(1, 0, 2, 3, 4).reshape(per_device, ny * nb * capacity, width)

    def from_rows(a):
        return a.reshape(per_device, ny, nb, capacity, width).transpose(1, 0, 2, 3, 4)

    x_rows = to_rows(lax.all_to_all(send_x, "ey", 0, 0, tiled=True))
    gate_up = jnp.einsum("jrd,jdf->jrf", x_rows, w_gate_up, preferred_element_type=jnp.float32)
    gate_half, up_half, sigmoid_part = swish_parts(gate_up, hidden_units)
    swish = gate_half * sigmoid_part
    hidden = (swish * up_half).astype(jnp.bfloat16)
    out_rows = jnp.einsum(
        "jrf,jfd->jrd", hidden, w_down, preferred_element_type=jnp.float32
    ).astype(jnp.bfloat16)
    back_out = lax.all_to_all(from_rows(out_rows), "ey", 0, 0, tiled=True)

    grad_rows = to_rows(lax.all_to_all(send_g, "ey", 0, 0, tiled=True))
    grad_hidden = jnp.einsum("jrd,jfd->jrf", grad_rows, w_down, preferred_element_type=jnp.float32)
    grad_gate = grad_hidden * up_half * sigmoid_part * (1.0 + gate_half * (1.0 - sigmoid_part))
    grad_up = grad_hidden * swish
    grad_act = jnp.concatenate([grad_gate, grad_up], axis=2).astype(jnp.bfloat16)
    grad_in = jnp.einsum(
        "jrf,jdf->jrd", grad_act, w_gate_up, preferred_element_type=jnp.float32
    ).astype(jnp.bfloat16)
    back_in = lax.all_to_all(from_rows(grad_in), "ey", 0, 0, tiled=True)

    back_f = back_out.astype(jnp.float32)
    row_inner = jnp.sum(back_f * routed_dy, axis=4)
    gate_part = jnp.sum(sel_f * row_inner[..., None], axis=(0, 1, 3)).reshape(nb, token_count, top_count)
    mixed_part = jnp.einsum(
        "yjoct,yjocd->otd",
        sel_tok.astype(jnp.float32),
        row_gate[..., None] * back_f,
        precision=lax.Precision.HIGHEST,
        preferred_element_type=jnp.float32,
    )
    tokens_part = jnp.einsum("yjoct,yjocd->otd", sel_tok, back_in, preferred_element_type=jnp.float32)
    gate_parts = [p.astype(jnp.float32) for p in split3(gate_part)]
    (both,) = ring_reduce(
        (jnp.concatenate([mixed_part, tokens_part] + gate_parts, axis=2),), "ez", nz, (jnp.bfloat16,)
    )
    mixed = both[:, :width]
    grad_tokens = both[:, width : 2 * width]
    grad_gates = join3(both[:, 2 * width :], top_count)

    down_local = jnp.einsum("jrf,jrd->jfd", hidden, grad_rows, preferred_element_type=jnp.float32)
    gate_up_local = jnp.einsum("jrd,jrf->jdf", x_rows, grad_act, preferred_element_type=jnp.float32)
    grad_gate_up = lax.psum_scatter(
        gate_up_local.astype(jnp.bfloat16), "dp", scatter_dimension=1, tiled=True
    ).astype(jnp.float32)
    grad_down = lax.psum_scatter(
        down_local.astype(jnp.bfloat16), "dp", scatter_dimension=2, tiled=True
    ).astype(jnp.float32)
    return (
        mixed.astype(jnp.bfloat16),
        grad_tokens.astype(jnp.bfloat16),
        grad_gates,
        grad_gate_up,
        grad_down,
    )


def solution(mesh):
    ny = mesh.devices.shape[1] // 8 if mesh.devices.shape[1] % 8 == 0 else 1
    nz = mesh.devices.shape[1] // ny
    split = Mesh(mesh.devices.reshape(mesh.devices.shape[0], ny, nz), ("dp", "ey", "ez"))
    rows = ("dp", "ey", "ez")
    experts = ("ey", "ez")
    in_specs = (
        P(rows, None),
        P(rows, None),
        P(rows, None),
        P(rows, None),
        P(experts, None, None),
        P(experts, None, None),
    )
    out_specs = (
        P(rows, None),
        P(rows, None),
        P(rows, None),
        P(experts, "dp", None),
        P(experts, None, "dp"),
    )
    return jax.shard_map(body, mesh=split, in_specs=in_specs, out_specs=out_specs, check_vma=False)
```

```python
import jax
import jax.numpy as jnp
from jax import lax
from jax.sharding import Mesh
from jax.sharding import PartitionSpec as P


def swish_parts(gate_up, hidden_units):
    gate_half = gate_up[..., :hidden_units]
    up_half = gate_up[..., hidden_units:]
    sigmoid_part = jax.nn.sigmoid(gate_half)
    return (gate_half, up_half, sigmoid_part)


def split3(x):
    hi = lax.reduce_precision(x, exponent_bits=8, mantissa_bits=7)
    rest = x - hi
    mid = lax.reduce_precision(rest, exponent_bits=8, mantissa_bits=7)
    lo = rest - mid
    return [p.astype(jnp.bfloat16) for p in (hi, mid, lo)]


def join3(parts, width):
    parts = parts.astype(jnp.float32)
    return (parts[..., :width] + parts[..., width : 2 * width]) + parts[..., 2 * width : 3 * width]


def spread(a, axis, n, sign):
    out = [a[0]]
    for k in range(1, n):
        out.append(lax.ppermute(a[k], axis, [(i, (i + sign * k) % n) for i in range(n)]))
    return jnp.stack(out)


def ring_offsets(n):
    half = n // 2
    return list(range(-half, n - half))


def ring_gather(x, axis, n):
    right = [(i, (i + 1) % n) for i in range(n)]
    left = [(i, (i - 1) % n) for i in range(n)]
    half = n // 2
    got = {0: x}
    fwd, bwd = x, x
    for k in range(1, half + 1):
        fwd = lax.ppermute(fwd, axis, right)
        got[-k] = fwd
        if k <= n - half - 1:
            bwd = lax.ppermute(bwd, axis, left)
            got[k] = bwd
    return jax.tree.map(lambda *xs: jnp.stack(xs), *[got[o] for o in ring_offsets(n)])


def ring_reduce(parts, axis, n, send_dtypes):
    right = [(i, (i + 1) % n) for i in range(n)]
    left = [(i, (i - 1) % n) for i in range(n)]
    half = n // 2
    index = {o: i for i, o in enumerate(ring_offsets(n))}

    def pick(o):
        return tuple(p[index[o]] for p in parts)

    def send(acc, perm):
        sent = lax.ppermute(tuple(a.astype(t) for a, t in zip(acc, send_dtypes)), axis, perm)
        return tuple(s.astype(jnp.float32) for s in sent)

    def add(a, b):
        return tuple(x + y for x, y in zip(a, b))

    total = pick(0)
    acc = pick(-half)
    for t in range(1, half):
        acc = add(send(acc, left), pick(-half + t))
    total = add(total, send(acc, left))
    m = n - half - 1
    if m > 0:
        acc = pick(m)
        for t in range(1, m):
            acc = add(send(acc, right), pick(m - t))
        total = add(total, send(acc, right))
    return total


def body(tokens, expert_ids, gate_weights, grad_output, w_gate_up, w_down):
    token_count, top_count = expert_ids.shape
    width = tokens.shape[1]
    per_device = w_gate_up.shape[0]
    hidden_units = w_down.shape[1]
    ny = lax.axis_size("ey")
    nz = lax.axis_size("ez")
    expert_total = ny * nz * per_device
    capacity = min(token_count, 2 * token_count * top_count // expert_total)
    pair_count = token_count * top_count
    my_z = lax.axis_index("ez")

    packed = jnp.concatenate(
        [tokens, grad_output, expert_ids.astype(jnp.bfloat16)] + split3(gate_weights), axis=1
    )
    both_g = ring_gather(packed, "ez", nz)
    tok_g = both_g[..., :width]
    dy_g = both_g[..., width : 2 * width]
    nb = both_g.shape[0]
    meta_g = both_g[..., 2 * width :].astype(jnp.float32)
    ids_g = meta_g[..., :top_count].astype(jnp.int32).reshape(nb, pair_count)
    gates_g = join3(meta_g[..., top_count:], top_count).reshape(nb, pair_count)

    my_y = lax.axis_index("ey")
    dest = (
        (((my_y + jnp.arange(ny, dtype=jnp.int32)) % ny)[:, None] * nz + my_z) * per_device
        + jnp.arange(per_device, dtype=jnp.int32)[None, :]
    )
    onehot = ids_g[None, None, :, :] == dest[:, :, None, None]
    onehot_i = onehot.astype(jnp.int32)
    slots = jnp.cumsum(onehot_i, axis=3) - onehot_i
    slot_axis = jnp.arange(capacity, dtype=jnp.int32)
    sel = jnp.logical_and(onehot[:, :, :, None, :], slots[:, :, :, None, :] == slot_axis[:, None])
    sel_f = sel.astype(jnp.float32)
    row_gate = jnp.sum(sel_f * gates_g[None, None, :, None, :], axis=4)
    sel_tok = jnp.sum(
        sel.reshape(ny, per_device, nb, capacity, token_count, top_count).astype(jnp.bfloat16),
        axis=5,
    )
    send_x = jnp.einsum(
        "yjoct,otd->yjocd", sel_tok, tok_g, preferred_element_type=jnp.float32
    ).astype(jnp.bfloat16)
    routed_dy = jnp.einsum("yjoct,otd->yjocd", sel_tok, dy_g, preferred_element_type=jnp.float32)
    send_g = (row_gate[..., None] * routed_dy).astype(jnp.bfloat16)

    def to_rows(a):
        return a.transpose(1, 0, 2, 3, 4).reshape(per_device, ny * nb * capacity, width)

    def from_rows(a):
        return a.reshape(per_device, ny, nb, capacity, width).transpose(1, 0, 2, 3, 4)

    x_rows = to_rows(spread(send_x, "ey", ny, 1))
    gate_up = jnp.einsum("jrd,jdf->jrf", x_rows, w_gate_up, preferred_element_type=jnp.float32)
    gate_half, up_half, sigmoid_part = swish_parts(gate_up, hidden_units)
    swish = gate_half * sigmoid_part
    hidden = (swish * up_half).astype(jnp.bfloat16)
    out_rows = jnp.einsum(
        "jrf,jfd->jrd", hidden, w_down, preferred_element_type=jnp.float32
    ).astype(jnp.bfloat16)
    back_out = spread(from_rows(out_rows), "ey", ny, -1)

    grad_rows = to_rows(spread(send_g, "ey", ny, 1))
    grad_hidden = jnp.einsum("jrd,jfd->jrf", grad_rows, w_down, preferred_element_type=jnp.float32)
    grad_gate = grad_hidden * up_half * sigmoid_part * (1.0 + gate_half * (1.0 - sigmoid_part))
    grad_up = grad_hidden * swish
    grad_act = jnp.concatenate([grad_gate, grad_up], axis=2).astype(jnp.bfloat16)
    grad_in = jnp.einsum(
        "jrf,jdf->jrd", grad_act, w_gate_up, preferred_element_type=jnp.float32
    ).astype(jnp.bfloat16)
    back_in = spread(from_rows(grad_in), "ey", ny, -1)

    back_f = back_out.astype(jnp.float32)
    row_inner = jnp.sum(back_f * routed_dy, axis=4)
    gate_part = jnp.sum(sel_f * row_inner[..., None], axis=(0, 1, 3)).reshape(nb, token_count, top_count)
    mixed_part = jnp.einsum(
        "yjoct,yjocd->otd",
        sel_tok.astype(jnp.float32),
        row_gate[..., None] * back_f,
        precision=lax.Precision.HIGHEST,
        preferred_element_type=jnp.float32,
    )
    gate_parts = [p.astype(jnp.float32) for p in split3(gate_part)]
    (first,) = ring_reduce(
        (jnp.concatenate([mixed_part] + gate_parts, axis=2),), "ez", nz, (jnp.bfloat16,)
    )
    mixed = first[:, :width]
    grad_gates = join3(first[:, width:], top_count)
    tokens_part = jnp.einsum("yjoct,yjocd->otd", sel_tok, back_in, preferred_element_type=jnp.float32)
    (grad_tokens,) = ring_reduce((tokens_part,), "ez", nz, (jnp.bfloat16,))

    down_local = jnp.einsum("jrf,jrd->jfd", hidden, grad_rows, preferred_element_type=jnp.float32)
    gate_up_local = jnp.einsum("jrd,jrf->jdf", x_rows, grad_act, preferred_element_type=jnp.float32)
    grad_gate_up = lax.psum_scatter(
        gate_up_local.astype(jnp.bfloat16), "dp", scatter_dimension=1, tiled=True
    ).astype(jnp.float32)
    grad_down = lax.psum_scatter(
        down_local.astype(jnp.bfloat16), "dp", scatter_dimension=2, tiled=True
    ).astype(jnp.float32)
    return (
        mixed.astype(jnp.bfloat16),
        grad_tokens.astype(jnp.bfloat16),
        grad_gates,
        grad_gate_up,
        grad_down,
    )


def solution(mesh):
    ny = mesh.devices.shape[1] // 8 if mesh.devices.shape[1] % 8 == 0 else 1
    nz = mesh.devices.shape[1] // ny
    split = Mesh(mesh.devices.reshape(mesh.devices.shape[0], ny, nz), ("dp", "ey", "ez"))
    rows = ("dp", "ey", "ez")
    experts = ("ey", "ez")
    in_specs = (
        P(rows, None),
        P(rows, None),
        P(rows, None),
        P(rows, None),
        P(experts, None, None),
        P(experts, None, None),
    )
    out_specs = (
        P(rows, None),
        P(rows, None),
        P(rows, None),
        P(experts, "dp", None),
        P(experts, None, "dp"),
    )
    return jax.shard_map(body, mesh=split, in_specs=in_specs, out_specs=out_specs, check_vma=False)
```

```python
import jax
import jax.numpy as jnp
from jax import lax
from jax.sharding import Mesh
from jax.sharding import PartitionSpec as P


def swish_parts(gate_up, hidden_units):
    gate_half = gate_up[..., :hidden_units]
    up_half = gate_up[..., hidden_units:]
    sigmoid_part = jax.nn.sigmoid(gate_half)
    return (gate_half, up_half, sigmoid_part)


def split3(x):
    hi = lax.reduce_precision(x, exponent_bits=8, mantissa_bits=7)
    rest = x - hi
    mid = lax.reduce_precision(rest, exponent_bits=8, mantissa_bits=7)
    lo = rest - mid
    return [p.astype(jnp.bfloat16) for p in (hi, mid, lo)]


def join3(parts, width):
    parts = parts.astype(jnp.float32)
    return (parts[..., :width] + parts[..., width : 2 * width]) + parts[..., 2 * width : 3 * width]


def spread(a, axis, n, sign):
    out = [a[0]]
    for k in range(1, n):
        out.append(lax.ppermute(a[k], axis, [(i, (i + sign * k) % n) for i in range(n)]))
    return jnp.stack(out)


def ring_offsets(n):
    half = n // 2
    return list(range(-half, n - half))


def ring_gather(x, axis, n):
    right = [(i, (i + 1) % n) for i in range(n)]
    left = [(i, (i - 1) % n) for i in range(n)]
    half = n // 2
    got = {0: x}
    fwd, bwd = x, x
    for k in range(1, half + 1):
        fwd = lax.ppermute(fwd, axis, right)
        got[-k] = fwd
        if k <= n - half - 1:
            bwd = lax.ppermute(bwd, axis, left)
            got[k] = bwd
    return jax.tree.map(lambda *xs: jnp.stack(xs), *[got[o] for o in ring_offsets(n)])


def ring_reduce(parts, axis, n, send_dtypes):
    right = [(i, (i + 1) % n) for i in range(n)]
    left = [(i, (i - 1) % n) for i in range(n)]
    half = n // 2
    index = {o: i for i, o in enumerate(ring_offsets(n))}

    def pick(o):
        return tuple(p[index[o]] for p in parts)

    def send(acc, perm):
        sent = lax.ppermute(tuple(a.astype(t) for a, t in zip(acc, send_dtypes)), axis, perm)
        return tuple(s.astype(jnp.float32) for s in sent)

    def add(a, b):
        return tuple(x + y for x, y in zip(a, b))

    total = pick(0)
    acc = pick(-half)
    for t in range(1, half):
        acc = add(send(acc, left), pick(-half + t))
    total = add(total, send(acc, left))
    m = n - half - 1
    if m > 0:
        acc = pick(m)
        for t in range(1, m):
            acc = add(send(acc, right), pick(m - t))
        total = add(total, send(acc, right))
    return total


def body(tokens, expert_ids, gate_weights, grad_output, w_gate_up, w_down):
    token_count, top_count = expert_ids.shape
    width = tokens.shape[1]
    per_device = w_gate_up.shape[0]
    hidden_units = w_down.shape[1]
    ny = lax.axis_size("ey")
    nz = lax.axis_size("ez")
    expert_total = ny * nz * per_device
    capacity = min(token_count, 2 * token_count * top_count // expert_total)
    pair_count = token_count * top_count
    my_z = lax.axis_index("ez")

    packed = jnp.concatenate(
        [tokens, grad_output, expert_ids.astype(jnp.bfloat16)] + split3(gate_weights), axis=1
    )
    both_g = ring_gather(packed, "ez", nz)
    tok_g = both_g[..., :width]
    dy_g = both_g[..., width : 2 * width]
    nb = both_g.shape[0]
    meta_g = both_g[..., 2 * width :].astype(jnp.float32)
    ids_g = meta_g[..., :top_count].astype(jnp.int32).reshape(nb, pair_count)
    gates_g = join3(meta_g[..., top_count:], top_count).reshape(nb, pair_count)

    my_y = lax.axis_index("ey")
    dest = (
        (((my_y + jnp.arange(ny, dtype=jnp.int32)) % ny)[:, None] * nz + my_z) * per_device
        + jnp.arange(per_device, dtype=jnp.int32)[None, :]
    )
    onehot = ids_g[None, None, :, :] == dest[:, :, None, None]
    onehot_i = onehot.astype(jnp.int32)
    slots = jnp.cumsum(onehot_i, axis=3) - onehot_i
    slot_axis = jnp.arange(capacity, dtype=jnp.int32)
    sel = jnp.logical_and(onehot[:, :, :, None, :], slots[:, :, :, None, :] == slot_axis[:, None])
    sel_f = sel.astype(jnp.float32)
    row_gate = jnp.sum(sel_f * gates_g[None, None, :, None, :], axis=4)
    sel_tok = jnp.sum(
        sel.reshape(ny, per_device, nb, capacity, token_count, top_count).astype(jnp.bfloat16),
        axis=5,
    )
    send_x = jnp.einsum(
        "yjoct,otd->yjocd", sel_tok, tok_g, preferred_element_type=jnp.float32
    ).astype(jnp.bfloat16)
    routed_dy = jnp.einsum("yjoct,otd->yjocd", sel_tok, dy_g, preferred_element_type=jnp.float32)
    send_g = (row_gate[..., None] * routed_dy).astype(jnp.bfloat16)

    def to_rows(a):
        return a.transpose(1, 0, 2, 3, 4).reshape(per_device, ny * nb * capacity, width)

    def from_rows(a):
        return a.reshape(per_device, ny, nb, capacity, width).transpose(1, 0, 2, 3, 4)

    x_rows = to_rows(spread(send_x, "ey", ny, 1))
    with jax.named_scope("grad_send"):
        grad_rows = to_rows(spread(send_g, "ey", ny, 1))
    with jax.named_scope("fwd_math"):
        gate_up = jnp.einsum("jrd,jdf->jrf", x_rows, w_gate_up, preferred_element_type=jnp.float32)
        gate_half, up_half, sigmoid_part = swish_parts(gate_up, hidden_units)
        swish = gate_half * sigmoid_part
        hidden = (swish * up_half).astype(jnp.bfloat16)
        out_rows = jnp.einsum(
            "jrf,jfd->jrd", hidden, w_down, preferred_element_type=jnp.float32
        ).astype(jnp.bfloat16)
    out_rows, grad_rows = lax.optimization_barrier((out_rows, grad_rows))
    back_out = spread(from_rows(out_rows), "ey", ny, -1)

    with jax.named_scope("bwd_math"):
        grad_hidden = jnp.einsum("jrd,jfd->jrf", grad_rows, w_down, preferred_element_type=jnp.float32)
        grad_gate = grad_hidden * up_half * sigmoid_part * (1.0 + gate_half * (1.0 - sigmoid_part))
        grad_up = grad_hidden * swish
        grad_act = jnp.concatenate([grad_gate, grad_up], axis=2).astype(jnp.bfloat16)
        grad_in = jnp.einsum(
            "jrf,jdf->jrd", grad_act, w_gate_up, preferred_element_type=jnp.float32
        ).astype(jnp.bfloat16)
    back_f = back_out.astype(jnp.float32)
    row_inner = jnp.sum(back_f * routed_dy, axis=4)
    gate_part = jnp.sum(sel_f * row_inner[..., None], axis=(0, 1, 3)).reshape(nb, token_count, top_count)
    mixed_part = jnp.einsum(
        "yjoct,yjocd->otd",
        sel_tok.astype(jnp.float32),
        row_gate[..., None] * back_f,
        precision=lax.Precision.HIGHEST,
        preferred_element_type=jnp.float32,
    )
    gate_parts = [p.astype(jnp.float32) for p in split3(gate_part)]
    (first,) = ring_reduce(
        (jnp.concatenate([mixed_part] + gate_parts, axis=2),), "ez", nz, (jnp.bfloat16,)
    )
    mixed = first[:, :width]
    grad_gates = join3(first[:, width:], top_count)
    grad_in_rows, mixed, grad_gates = lax.optimization_barrier((from_rows(grad_in), mixed, grad_gates))
    back_in = spread(grad_in_rows, "ey", ny, -1)
    tokens_part = jnp.einsum("yjoct,yjocd->otd", sel_tok, back_in, preferred_element_type=jnp.float32)

    (grad_tokens,) = ring_reduce((tokens_part,), "ez", nz, (jnp.bfloat16,))

    down_local = jnp.einsum("jrf,jrd->jfd", hidden, grad_rows, preferred_element_type=jnp.float32)
    gate_up_local = jnp.einsum("jrd,jrf->jdf", x_rows, grad_act, preferred_element_type=jnp.float32)
    grad_gate_up = lax.psum_scatter(
        gate_up_local.astype(jnp.bfloat16), "dp", scatter_dimension=1, tiled=True
    ).astype(jnp.float32)
    grad_down = lax.psum_scatter(
        down_local.astype(jnp.bfloat16), "dp", scatter_dimension=2, tiled=True
    ).astype(jnp.float32)
    return (
        mixed.astype(jnp.bfloat16),
        grad_tokens.astype(jnp.bfloat16),
        grad_gates,
        grad_gate_up,
        grad_down,
    )


def solution(mesh):
    ny = mesh.devices.shape[1] // 8 if mesh.devices.shape[1] % 8 == 0 else 1
    nz = mesh.devices.shape[1] // ny
    split = Mesh(mesh.devices.reshape(mesh.devices.shape[0], ny, nz), ("dp", "ey", "ez"))
    rows = ("dp", "ey", "ez")
    experts = ("ey", "ez")
    in_specs = (
        P(rows, None),
        P(rows, None),
        P(rows, None),
        P(rows, None),
        P(experts, None, None),
        P(experts, None, None),
    )
    out_specs = (
        P(rows, None),
        P(rows, None),
        P(rows, None),
        P(experts, "dp", None),
        P(experts, None, "dp"),
    )
    return jax.shard_map(body, mesh=split, in_specs=in_specs, out_specs=out_specs, check_vma=False)
```

```python
import jax
import jax.numpy as jnp
from jax import lax
from jax.sharding import Mesh
from jax.sharding import PartitionSpec as P


def swish_parts(gate_up, hidden_units):
    gate_half = gate_up[..., :hidden_units]
    up_half = gate_up[..., hidden_units:]
    sigmoid_part = jax.nn.sigmoid(gate_half)
    return (gate_half, up_half, sigmoid_part)


def split3(x):
    hi = lax.reduce_precision(x, exponent_bits=8, mantissa_bits=7)
    rest = x - hi
    mid = lax.reduce_precision(rest, exponent_bits=8, mantissa_bits=7)
    lo = rest - mid
    return [p.astype(jnp.bfloat16) for p in (hi, mid, lo)]


def join3(parts, width):
    parts = parts.astype(jnp.float32)
    return (parts[..., :width] + parts[..., width : 2 * width]) + parts[..., 2 * width : 3 * width]


def spread(a, axis, n, sign):
    out = [a[0]]
    for k in range(1, n):
        out.append(lax.ppermute(a[k], axis, [(i, (i + sign * k) % n) for i in range(n)]))
    return jnp.stack(out)


def ring_offsets(n):
    half = n // 2
    return list(range(-half, n - half))


def ring_gather(x, axis, n):
    right = [(i, (i + 1) % n) for i in range(n)]
    left = [(i, (i - 1) % n) for i in range(n)]
    half = n // 2
    got = {0: x}
    fwd, bwd = x, x
    for k in range(1, half + 1):
        fwd = lax.ppermute(fwd, axis, right)
        got[-k] = fwd
        if k <= n - half - 1:
            bwd = lax.ppermute(bwd, axis, left)
            got[k] = bwd
    return jax.tree.map(lambda *xs: jnp.stack(xs), *[got[o] for o in ring_offsets(n)])


def ring_reduce(parts, axis, n, send_dtypes):
    right = [(i, (i + 1) % n) for i in range(n)]
    left = [(i, (i - 1) % n) for i in range(n)]
    half = n // 2
    index = {o: i for i, o in enumerate(ring_offsets(n))}

    def pick(o):
        return tuple(p[index[o]] for p in parts)

    def send(acc, perm):
        sent = lax.ppermute(tuple(a.astype(t) for a, t in zip(acc, send_dtypes)), axis, perm)
        return tuple(s.astype(jnp.float32) for s in sent)

    def add(a, b):
        return tuple(x + y for x, y in zip(a, b))

    total = pick(0)
    acc = pick(-half)
    for t in range(1, half):
        acc = add(send(acc, left), pick(-half + t))
    total = add(total, send(acc, left))
    m = n - half - 1
    if m > 0:
        acc = pick(m)
        for t in range(1, m):
            acc = add(send(acc, right), pick(m - t))
        total = add(total, send(acc, right))
    return total


def body(tokens, expert_ids, gate_weights, grad_output, w_gate_up, w_down):
    token_count, top_count = expert_ids.shape
    width = tokens.shape[1]
    per_device = w_gate_up.shape[0]
    hidden_units = w_down.shape[1]
    ny = lax.axis_size("ey")
    nz = lax.axis_size("ez")
    expert_total = ny * nz * per_device
    capacity = min(token_count, 2 * token_count * top_count // expert_total)
    pair_count = token_count * top_count
    my_z = lax.axis_index("ez")

    packed = jnp.concatenate([tokens, expert_ids.astype(jnp.bfloat16)] + split3(gate_weights), axis=1)
    tok_meta_g = ring_gather(packed, "ez", nz)
    dy_g = ring_gather(grad_output, "ez", nz)
    tok_g = tok_meta_g[..., :width]
    nb = tok_meta_g.shape[0]
    meta_g = tok_meta_g[..., width:].astype(jnp.float32)
    ids_g = meta_g[..., :top_count].astype(jnp.int32).reshape(nb, pair_count)
    gates_g = join3(meta_g[..., top_count:], top_count).reshape(nb, pair_count)

    my_y = lax.axis_index("ey")
    dest = (
        (((my_y + jnp.arange(ny, dtype=jnp.int32)) % ny)[:, None] * nz + my_z) * per_device
        + jnp.arange(per_device, dtype=jnp.int32)[None, :]
    )
    onehot = ids_g[None, None, :, :] == dest[:, :, None, None]
    onehot_i = onehot.astype(jnp.int32)
    slots = jnp.cumsum(onehot_i, axis=3) - onehot_i
    slot_axis = jnp.arange(capacity, dtype=jnp.int32)
    sel = jnp.logical_and(onehot[:, :, :, None, :], slots[:, :, :, None, :] == slot_axis[:, None])
    sel_f = sel.astype(jnp.float32)
    row_gate = jnp.sum(sel_f * gates_g[None, None, :, None, :], axis=4)
    sel_tok = jnp.sum(
        sel.reshape(ny, per_device, nb, capacity, token_count, top_count).astype(jnp.bfloat16),
        axis=5,
    )
    send_x = jnp.einsum(
        "yjoct,otd->yjocd", sel_tok, tok_g, preferred_element_type=jnp.float32
    ).astype(jnp.bfloat16)
    routed_dy = jnp.einsum("yjoct,otd->yjocd", sel_tok, dy_g, preferred_element_type=jnp.float32)
    send_g = (row_gate[..., None] * routed_dy).astype(jnp.bfloat16)

    def to_rows(a):
        return a.transpose(1, 0, 2, 3, 4).reshape(per_device, ny * nb * capacity, width)

    def from_rows(a):
        return a.reshape(per_device, ny, nb, capacity, width).transpose(1, 0, 2, 3, 4)

    x_rows = to_rows(spread(send_x, "ey", ny, 1))
    gate_up = jnp.einsum("jrd,jdf->jrf", x_rows, w_gate_up, preferred_element_type=jnp.float32)
    gate_half, up_half, sigmoid_part = swish_parts(gate_up, hidden_units)
    swish = gate_half * sigmoid_part
    hidden = (swish * up_half).astype(jnp.bfloat16)
    out_rows = jnp.einsum(
        "jrf,jfd->jrd", hidden, w_down, preferred_element_type=jnp.float32
    ).astype(jnp.bfloat16)
    back_out = spread(from_rows(out_rows), "ey", ny, -1)

    grad_rows = to_rows(spread(send_g, "ey", ny, 1))
    grad_hidden = jnp.einsum("jrd,jfd->jrf", grad_rows, w_down, preferred_element_type=jnp.float32)
    grad_gate = grad_hidden * up_half * sigmoid_part * (1.0 + gate_half * (1.0 - sigmoid_part))
    grad_up = grad_hidden * swish
    grad_act = jnp.concatenate([grad_gate, grad_up], axis=2).astype(jnp.bfloat16)
    grad_in = jnp.einsum(
        "jrf,jdf->jrd", grad_act, w_gate_up, preferred_element_type=jnp.float32
    ).astype(jnp.bfloat16)
    back_in = spread(from_rows(grad_in), "ey", ny, -1)

    back_f = back_out.astype(jnp.float32)
    row_inner = jnp.sum(back_f * routed_dy, axis=4)
    gate_part = jnp.sum(sel_f * row_inner[..., None], axis=(0, 1, 3)).reshape(nb, token_count, top_count)
    mixed_part = jnp.einsum(
        "yjoct,yjocd->otd",
        sel_tok.astype(jnp.float32),
        row_gate[..., None] * back_f,
        precision=lax.Precision.HIGHEST,
        preferred_element_type=jnp.float32,
    )
    gate_parts = [p.astype(jnp.float32) for p in split3(gate_part)]
    (first,) = ring_reduce(
        (jnp.concatenate([mixed_part] + gate_parts, axis=2),), "ez", nz, (jnp.bfloat16,)
    )
    mixed = first[:, :width]
    grad_gates = join3(first[:, width:], top_count)
    tokens_part = jnp.einsum("yjoct,yjocd->otd", sel_tok, back_in, preferred_element_type=jnp.float32)
    (grad_tokens,) = ring_reduce((tokens_part,), "ez", nz, (jnp.bfloat16,))

    down_local = jnp.einsum("jrf,jrd->jfd", hidden, grad_rows, preferred_element_type=jnp.float32)
    gate_up_local = jnp.einsum("jrd,jrf->jdf", x_rows, grad_act, preferred_element_type=jnp.float32)
    grad_gate_up = lax.psum_scatter(
        gate_up_local.astype(jnp.bfloat16), "dp", scatter_dimension=1, tiled=True
    ).astype(jnp.float32)
    grad_down = lax.psum_scatter(
        down_local.astype(jnp.bfloat16), "dp", scatter_dimension=2, tiled=True
    ).astype(jnp.float32)
    return (
        mixed.astype(jnp.bfloat16),
        grad_tokens.astype(jnp.bfloat16),
        grad_gates,
        grad_gate_up,
        grad_down,
    )


def solution(mesh):
    ny = mesh.devices.shape[1] // 8 if mesh.devices.shape[1] % 8 == 0 else 1
    nz = mesh.devices.shape[1] // ny
    split = Mesh(mesh.devices.reshape(mesh.devices.shape[0], ny, nz), ("dp", "ey", "ez"))
    rows = ("dp", "ey", "ez")
    experts = ("ey", "ez")
    in_specs = (
        P(rows, None),
        P(rows, None),
        P(rows, None),
        P(rows, None),
        P(experts, None, None),
        P(experts, None, None),
    )
    out_specs = (
        P(rows, None),
        P(rows, None),
        P(rows, None),
        P(experts, "dp", None),
        P(experts, None, "dp"),
    )
    return jax.shard_map(body, mesh=split, in_specs=in_specs, out_specs=out_specs, check_vma=False)
```

```python
import jax
import jax.numpy as jnp
from jax import lax
from jax.sharding import Mesh
from jax.sharding import PartitionSpec as P


def swish_parts(gate_up, hidden_units):
    gate_half = gate_up[..., :hidden_units]
    up_half = gate_up[..., hidden_units:]
    sigmoid_part = jax.nn.sigmoid(gate_half)
    return (gate_half, up_half, sigmoid_part)


def split3(x):
    hi = lax.reduce_precision(x, exponent_bits=8, mantissa_bits=7)
    rest = x - hi
    mid = lax.reduce_precision(rest, exponent_bits=8, mantissa_bits=7)
    lo = rest - mid
    return [p.astype(jnp.bfloat16) for p in (hi, mid, lo)]


def join3(parts, width):
    parts = parts.astype(jnp.float32)
    return (parts[..., :width] + parts[..., width : 2 * width]) + parts[..., 2 * width : 3 * width]


def spread(a, axis, n, sign):
    out = [a[0]]
    for k in range(1, n):
        out.append(lax.ppermute(a[k], axis, [(i, (i + sign * k) % n) for i in range(n)]))
    return jnp.stack(out)


def ring_offsets(n):
    half = n // 2
    return list(range(-half, n - half))


def ring_gather(x, axis, n):
    right = [(i, (i + 1) % n) for i in range(n)]
    left = [(i, (i - 1) % n) for i in range(n)]
    half = n // 2
    got = {0: x}
    fwd, bwd = x, x
    for k in range(1, half + 1):
        fwd = lax.ppermute(fwd, axis, right)
        got[-k] = fwd
        if k <= n - half - 1:
            bwd = lax.ppermute(bwd, axis, left)
            got[k] = bwd
    return jax.tree.map(lambda *xs: jnp.stack(xs), *[got[o] for o in ring_offsets(n)])


def ring_reduce(parts, axis, n, send_dtypes):
    right = [(i, (i + 1) % n) for i in range(n)]
    left = [(i, (i - 1) % n) for i in range(n)]
    half = n // 2
    index = {o: i for i, o in enumerate(ring_offsets(n))}

    def pick(o):
        return tuple(p[index[o]] for p in parts)

    def send(acc, perm):
        sent = lax.ppermute(tuple(a.astype(t) for a, t in zip(acc, send_dtypes)), axis, perm)
        return tuple(s.astype(jnp.float32) for s in sent)

    def add(a, b):
        return tuple(x + y for x, y in zip(a, b))

    total = pick(0)
    acc = pick(-half)
    for t in range(1, half):
        acc = add(send(acc, left), pick(-half + t))
    total = add(total, send(acc, left))
    m = n - half - 1
    if m > 0:
        acc = pick(m)
        for t in range(1, m):
            acc = add(send(acc, right), pick(m - t))
        total = add(total, send(acc, right))
    return total


def body(tokens, expert_ids, gate_weights, grad_output, w_gate_up, w_down):
    token_count, top_count = expert_ids.shape
    width = tokens.shape[1]
    per_device = w_gate_up.shape[0]
    hidden_units = w_down.shape[1]
    ny = lax.axis_size("ey")
    nz = lax.axis_size("ez")
    expert_total = ny * nz * per_device
    capacity = min(token_count, 2 * token_count * top_count // expert_total)
    pair_count = token_count * top_count
    my_z = lax.axis_index("ez")

    packed = jnp.concatenate(
        [tokens, grad_output, expert_ids.astype(jnp.bfloat16)] + split3(gate_weights), axis=1
    )
    both_g = ring_gather(packed, "ez", nz)
    tok_g = both_g[..., :width]
    dy_g = both_g[..., width : 2 * width]
    nb = both_g.shape[0]
    meta_g = both_g[..., 2 * width :].astype(jnp.float32)
    ids_g = meta_g[..., :top_count].astype(jnp.int32).reshape(nb, pair_count)
    gates_g = join3(meta_g[..., top_count:], top_count).reshape(nb, pair_count)

    my_y = lax.axis_index("ey")
    dest = (
        (((my_y + jnp.arange(ny, dtype=jnp.int32)) % ny)[:, None] * nz + my_z) * per_device
        + jnp.arange(per_device, dtype=jnp.int32)[None, :]
    )
    onehot = ids_g[None, None, :, :] == dest[:, :, None, None]
    onehot_i = onehot.astype(jnp.int32)
    slots = jnp.cumsum(onehot_i, axis=3) - onehot_i
    slot_axis = jnp.arange(capacity, dtype=jnp.int32)
    sel = jnp.logical_and(onehot[:, :, :, None, :], slots[:, :, :, None, :] == slot_axis[:, None])
    sel_f = sel.astype(jnp.float32)
    row_gate = jnp.sum(sel_f * gates_g[None, None, :, None, :], axis=4)
    sel_tok = jnp.sum(
        sel.reshape(ny, per_device, nb, capacity, token_count, top_count).astype(jnp.bfloat16),
        axis=5,
    )
    send_x = jnp.einsum(
        "yjoct,otd->yjocd", sel_tok, tok_g, preferred_element_type=jnp.float32
    ).astype(jnp.bfloat16)
    routed_dy = jnp.einsum("yjoct,otd->yjocd", sel_tok, dy_g, preferred_element_type=jnp.float32)
    send_g = (row_gate[..., None] * routed_dy).astype(jnp.bfloat16)

    def to_rows(a):
        return a.transpose(1, 0, 2, 3, 4).reshape(per_device, ny * nb * capacity, a.shape[-1])

    def from_rows(a):
        return a.reshape(per_device, ny, nb, capacity, a.shape[-1]).transpose(1, 0, 2, 3, 4)

    arrived = to_rows(spread(jnp.concatenate([send_x, send_g], axis=-1), "ey", ny, 1))
    x_rows = arrived[..., :width]
    grad_rows = arrived[..., width:]
    gate_up = jnp.einsum("jrd,jdf->jrf", x_rows, w_gate_up, preferred_element_type=jnp.float32)
    gate_half, up_half, sigmoid_part = swish_parts(gate_up, hidden_units)
    swish = gate_half * sigmoid_part
    hidden = (swish * up_half).astype(jnp.bfloat16)
    out_rows = jnp.einsum(
        "jrf,jfd->jrd", hidden, w_down, preferred_element_type=jnp.float32
    ).astype(jnp.bfloat16)

    grad_hidden = jnp.einsum("jrd,jfd->jrf", grad_rows, w_down, preferred_element_type=jnp.float32)
    grad_gate = grad_hidden * up_half * sigmoid_part * (1.0 + gate_half * (1.0 - sigmoid_part))
    grad_up = grad_hidden * swish
    grad_act = jnp.concatenate([grad_gate, grad_up], axis=2).astype(jnp.bfloat16)
    grad_in = jnp.einsum(
        "jrf,jdf->jrd", grad_act, w_gate_up, preferred_element_type=jnp.float32
    ).astype(jnp.bfloat16)
    back = spread(from_rows(jnp.concatenate([out_rows, grad_in], axis=-1)), "ey", ny, -1)
    back_out = back[..., :width]
    back_in = back[..., width:]

    back_f = back_out.astype(jnp.float32)
    row_inner = jnp.sum(back_f * routed_dy, axis=4)
    gate_part = jnp.sum(sel_f * row_inner[..., None], axis=(0, 1, 3)).reshape(nb, token_count, top_count)
    mixed_part = jnp.einsum(
        "yjoct,yjocd->otd",
        sel_tok.astype(jnp.float32),
        row_gate[..., None] * back_f,
        precision=lax.Precision.HIGHEST,
        preferred_element_type=jnp.float32,
    )
    gate_parts = [p.astype(jnp.float32) for p in split3(gate_part)]
    (first,) = ring_reduce(
        (jnp.concatenate([mixed_part] + gate_parts, axis=2),), "ez", nz, (jnp.bfloat16,)
    )
    mixed = first[:, :width]
    grad_gates = join3(first[:, width:], top_count)
    tokens_part = jnp.einsum("yjoct,yjocd->otd", sel_tok, back_in, preferred_element_type=jnp.float32)
    (grad_tokens,) = ring_reduce((tokens_part,), "ez", nz, (jnp.bfloat16,))

    down_local = jnp.einsum("jrf,jrd->jfd", hidden, grad_rows, preferred_element_type=jnp.float32)
    gate_up_local = jnp.einsum("jrd,jrf->jdf", x_rows, grad_act, preferred_element_type=jnp.float32)
    grad_gate_up = lax.psum_scatter(
        gate_up_local.astype(jnp.bfloat16), "dp", scatter_dimension=1, tiled=True
    ).astype(jnp.float32)
    grad_down = lax.psum_scatter(
        down_local.astype(jnp.bfloat16), "dp", scatter_dimension=2, tiled=True
    ).astype(jnp.float32)
    return (
        mixed.astype(jnp.bfloat16),
        grad_tokens.astype(jnp.bfloat16),
        grad_gates,
        grad_gate_up,
        grad_down,
    )


def solution(mesh):
    ny = mesh.devices.shape[1] // 8 if mesh.devices.shape[1] % 8 == 0 else 1
    nz = mesh.devices.shape[1] // ny
    split = Mesh(mesh.devices.reshape(mesh.devices.shape[0], ny, nz), ("dp", "ey", "ez"))
    rows = ("dp", "ey", "ez")
    experts = ("ey", "ez")
    in_specs = (
        P(rows, None),
        P(rows, None),
        P(rows, None),
        P(rows, None),
        P(experts, None, None),
        P(experts, None, None),
    )
    out_specs = (
        P(rows, None),
        P(rows, None),
        P(rows, None),
        P(experts, "dp", None),
        P(experts, None, "dp"),
    )
    return jax.shard_map(body, mesh=split, in_specs=in_specs, out_specs=out_specs, check_vma=False)
```

```python
import jax
import jax.numpy as jnp
from jax import lax
from jax.sharding import Mesh
from jax.sharding import PartitionSpec as P


def swish_parts(gate_up, hidden_units):
    gate_half = gate_up[..., :hidden_units]
    up_half = gate_up[..., hidden_units:]
    sigmoid_part = jax.nn.sigmoid(gate_half)
    return (gate_half, up_half, sigmoid_part)


def split3(x):
    hi = lax.reduce_precision(x, exponent_bits=8, mantissa_bits=7)
    rest = x - hi
    mid = lax.reduce_precision(rest, exponent_bits=8, mantissa_bits=7)
    lo = rest - mid
    return [p.astype(jnp.bfloat16) for p in (hi, mid, lo)]


def join3(parts, width):
    parts = parts.astype(jnp.float32)
    return (parts[..., :width] + parts[..., width : 2 * width]) + parts[..., 2 * width : 3 * width]


def spread(a, axis, n, sign):
    out = [a[0]]
    for k in range(1, n):
        perm = [(i, (i + sign * k) % n) for i in range(n)]
        halves = jnp.split(a[k], 2, axis=1)
        out.append(jnp.concatenate([lax.ppermute(h, axis, perm) for h in halves], axis=1))
    return jnp.stack(out)


def ring_offsets(n):
    half = n // 2
    return list(range(-half, n - half))


def ring_gather(x, axis, n):
    right = [(i, (i + 1) % n) for i in range(n)]
    left = [(i, (i - 1) % n) for i in range(n)]
    half = n // 2
    got = {0: x}
    fwd, bwd = x, x
    for k in range(1, half + 1):
        fwd = lax.ppermute(fwd, axis, right)
        got[-k] = fwd
        if k <= n - half - 1:
            bwd = lax.ppermute(bwd, axis, left)
            got[k] = bwd
    return jax.tree.map(lambda *xs: jnp.stack(xs), *[got[o] for o in ring_offsets(n)])


def ring_reduce(parts, axis, n, send_dtypes):
    right = [(i, (i + 1) % n) for i in range(n)]
    left = [(i, (i - 1) % n) for i in range(n)]
    half = n // 2
    index = {o: i for i, o in enumerate(ring_offsets(n))}

    def pick(o):
        return tuple(p[index[o]] for p in parts)

    def send(acc, perm):
        sent = lax.ppermute(tuple(a.astype(t) for a, t in zip(acc, send_dtypes)), axis, perm)
        return tuple(s.astype(jnp.float32) for s in sent)

    def add(a, b):
        return tuple(x + y for x, y in zip(a, b))

    total = pick(0)
    acc = pick(-half)
    for t in range(1, half):
        acc = add(send(acc, left), pick(-half + t))
    total = add(total, send(acc, left))
    m = n - half - 1
    if m > 0:
        acc = pick(m)
        for t in range(1, m):
            acc = add(send(acc, right), pick(m - t))
        total = add(total, send(acc, right))
    return total


def body(tokens, expert_ids, gate_weights, grad_output, w_gate_up, w_down):
    token_count, top_count = expert_ids.shape
    width = tokens.shape[1]
    per_device = w_gate_up.shape[0]
    hidden_units = w_down.shape[1]
    ny = lax.axis_size("ey")
    nz = lax.axis_size("ez")
    expert_total = ny * nz * per_device
    capacity = min(token_count, 2 * token_count * top_count // expert_total)
    pair_count = token_count * top_count
    my_z = lax.axis_index("ez")

    packed = jnp.concatenate(
        [tokens, grad_output, expert_ids.astype(jnp.bfloat16)] + split3(gate_weights), axis=1
    )
    both_g = ring_gather(packed, "ez", nz)
    tok_g = both_g[..., :width]
    dy_g = both_g[..., width : 2 * width]
    nb = both_g.shape[0]
    meta_g = both_g[..., 2 * width :].astype(jnp.float32)
    ids_g = meta_g[..., :top_count].astype(jnp.int32).reshape(nb, pair_count)
    gates_g = join3(meta_g[..., top_count:], top_count).reshape(nb, pair_count)

    my_y = lax.axis_index("ey")
    dest = (
        (((my_y + jnp.arange(ny, dtype=jnp.int32)) % ny)[:, None] * nz + my_z) * per_device
        + jnp.arange(per_device, dtype=jnp.int32)[None, :]
    )
    onehot = ids_g[None, None, :, :] == dest[:, :, None, None]
    onehot_i = onehot.astype(jnp.int32)
    slots = jnp.cumsum(onehot_i, axis=3) - onehot_i
    slot_axis = jnp.arange(capacity, dtype=jnp.int32)
    sel = jnp.logical_and(onehot[:, :, :, None, :], slots[:, :, :, None, :] == slot_axis[:, None])
    sel_f = sel.astype(jnp.float32)
    row_gate = jnp.sum(sel_f * gates_g[None, None, :, None, :], axis=4)
    sel_tok = jnp.sum(
        sel.reshape(ny, per_device, nb, capacity, token_count, top_count).astype(jnp.bfloat16),
        axis=5,
    )
    send_x = jnp.einsum(
        "yjoct,otd->yjocd", sel_tok, tok_g, preferred_element_type=jnp.float32
    ).astype(jnp.bfloat16)
    routed_dy = jnp.einsum("yjoct,otd->yjocd", sel_tok, dy_g, preferred_element_type=jnp.float32)
    send_g = (row_gate[..., None] * routed_dy).astype(jnp.bfloat16)

    def to_rows(a):
        return a.transpose(1, 0, 2, 3, 4).reshape(per_device, ny * nb * capacity, width)

    def from_rows(a):
        return a.reshape(per_device, ny, nb, capacity, width).transpose(1, 0, 2, 3, 4)

    x_rows = to_rows(spread(send_x, "ey", ny, 1))
    gate_up = jnp.einsum("jrd,jdf->jrf", x_rows, w_gate_up, preferred_element_type=jnp.float32)
    gate_half, up_half, sigmoid_part = swish_parts(gate_up, hidden_units)
    swish = gate_half * sigmoid_part
    hidden = (swish * up_half).astype(jnp.bfloat16)
    out_rows = jnp.einsum(
        "jrf,jfd->jrd", hidden, w_down, preferred_element_type=jnp.float32
    ).astype(jnp.bfloat16)
    back_out = spread(from_rows(out_rows), "ey", ny, -1)

    grad_rows = to_rows(spread(send_g, "ey", ny, 1))
    grad_hidden = jnp.einsum("jrd,jfd->jrf", grad_rows, w_down, preferred_element_type=jnp.float32)
    grad_gate = grad_hidden * up_half * sigmoid_part * (1.0 + gate_half * (1.0 - sigmoid_part))
    grad_up = grad_hidden * swish
    grad_act = jnp.concatenate([grad_gate, grad_up], axis=2).astype(jnp.bfloat16)
    grad_in = jnp.einsum(
        "jrf,jdf->jrd", grad_act, w_gate_up, preferred_element_type=jnp.float32
    ).astype(jnp.bfloat16)
    back_in = spread(from_rows(grad_in), "ey", ny, -1)

    back_f = back_out.astype(jnp.float32)
    row_inner = jnp.sum(back_f * routed_dy, axis=4)
    gate_part = jnp.sum(sel_f * row_inner[..., None], axis=(0, 1, 3)).reshape(nb, token_count, top_count)
    mixed_part = jnp.einsum(
        "yjoct,yjocd->otd",
        sel_tok.astype(jnp.float32),
        row_gate[..., None] * back_f,
        precision=lax.Precision.HIGHEST,
        preferred_element_type=jnp.float32,
    )
    gate_parts = [p.astype(jnp.float32) for p in split3(gate_part)]
    (first,) = ring_reduce(
        (jnp.concatenate([mixed_part] + gate_parts, axis=2),), "ez", nz, (jnp.bfloat16,)
    )
    mixed = first[:, :width]
    grad_gates = join3(first[:, width:], top_count)
    tokens_part = jnp.einsum("yjoct,yjocd->otd", sel_tok, back_in, preferred_element_type=jnp.float32)
    (grad_tokens,) = ring_reduce((tokens_part,), "ez", nz, (jnp.bfloat16,))

    down_local = jnp.einsum("jrf,jrd->jfd", hidden, grad_rows, preferred_element_type=jnp.float32)
    gate_up_local = jnp.einsum("jrd,jrf->jdf", x_rows, grad_act, preferred_element_type=jnp.float32)
    grad_gate_up = lax.psum_scatter(
        gate_up_local.astype(jnp.bfloat16), "dp", scatter_dimension=1, tiled=True
    ).astype(jnp.float32)
    grad_down = lax.psum_scatter(
        down_local.astype(jnp.bfloat16), "dp", scatter_dimension=2, tiled=True
    ).astype(jnp.float32)
    return (
        mixed.astype(jnp.bfloat16),
        grad_tokens.astype(jnp.bfloat16),
        grad_gates,
        grad_gate_up,
        grad_down,
    )


def solution(mesh):
    ny = mesh.devices.shape[1] // 8 if mesh.devices.shape[1] % 8 == 0 else 1
    nz = mesh.devices.shape[1] // ny
    split = Mesh(mesh.devices.reshape(mesh.devices.shape[0], ny, nz), ("dp", "ey", "ez"))
    rows = ("dp", "ey", "ez")
    experts = ("ey", "ez")
    in_specs = (
        P(rows, None),
        P(rows, None),
        P(rows, None),
        P(rows, None),
        P(experts, None, None),
        P(experts, None, None),
    )
    out_specs = (
        P(rows, None),
        P(rows, None),
        P(rows, None),
        P(experts, "dp", None),
        P(experts, None, "dp"),
    )
    return jax.shard_map(body, mesh=split, in_specs=in_specs, out_specs=out_specs, check_vma=False)
```
